256 devices in a mesh: win: 4 (over z_lo), rcv: 64 (over x, z_hi, y, core).
Axes of the slice: x: 4, y: 4, z: 8 (z_hi: 2, z_lo: 4; z = z_hi * 4 + z_lo), core: 2. Of those that a mesh axis runs over, the one named last changes fastest.
Arguments:
- spectra: bfloat16 [4096, 16, 2, 1024], P('rcv', 'win'), may hold values from -6 to 6
- source_block: int32 [1], replicated, may hold values from 0 to 63
Outputs:
- correlations: bfloat16 [4096, 64, 2048], P('rcv', None, 'win')
The draws below stay inside these ranges and needn't reach their ends.
All inputs are finite; a program needn't handle non-finite values.
Results may differ from the reference program's by a relative error of at most 0.015.
Values may be sent and summed in bfloat16 or wider, within the bound.
No kernel may reach another device: no remote copies, remote signals or barrier semaphores. Data moves between devices by JAX's collectives and lax.ppermute only.
A program may use at most 256 MiB of HBM per device.

```python
import jax
import jax.numpy as jnp
from jax import lax

FREQS = 1024
LAGS = 2048
WINDOWS = 16
CH_DEV = 64
SOURCES = 64
CHANNELS = 4096
N_RCV = 64


def block_levels(rng, shape, split, least, top_value):
    level = 1.0
    for position, shards_of in split:
        draws = jax.random.uniform(jax.random.fold_in(jax.random.fold_in(rng, 6), position), (shards_of,), jnp.float32, least / len(split), top_value / len(split))
        level = level * jnp.repeat(jnp.exp(draws), shape[position] // shards_of).reshape((-1,) + (1,) * (len(shape) - 1 - position))
    return level


def centred(own_key, shape, width, limit, cuts=(), held_as=jnp.bfloat16):
    entries = jax.random.normal(own_key, shape, jnp.float32) * width
    if len(cuts) > 0:
        entries = block_levels(own_key, shape, cuts, -0.22, 0.18) * entries
    return jnp.clip(entries, min=-limit, max=limit).astype(held_as)


def setup_inputs(seed: int = 0) -> dict:
    key_of = jax.random.split(jax.random.key(seed), 3)
    return {
        "spectra": centred(key_of[0], (CHANNELS, WINDOWS, 2, FREQS), 1.0, 6.0, ((0, 64), (1, 4))),
        "source_block": jax.random.randint(key_of[1], (1,), 0, N_RCV).astype(jnp.int32),
    }


def cross_block(receivers, source):
    flipped = jnp.stack([-receivers[:, :, 1], receivers[:, :, 0]], axis=2)
    real_part = jnp.einsum('rwcf,swcf->rsf', receivers, source)
    imag_part = jnp.einsum('rwcf,swcf->rsf', flipped, source)
    return (real_part, imag_part)

def reference(spectra, source_block):
    first_row = (source_block[0] * CH_DEV).astype(jnp.int32)
    source = lax.dynamic_slice_in_dim(spectra, first_row, SOURCES, 0).astype(jnp.float32)
    blocks = spectra.reshape(N_RCV, CH_DEV, WINDOWS, 2, FREQS)
    lag_scale = 1.0 / jnp.sqrt(jnp.float32(LAGS * WINDOWS))

    def per_block(receivers):
        real_part, imag_part = cross_block(receivers.astype(jnp.float32), source)
        real_part = lax.optimization_barrier(real_part.astype(jnp.bfloat16)).astype(jnp.float32)
        imag_part = lax.optimization_barrier(imag_part.astype(jnp.bfloat16)).astype(jnp.float32)
        spectrum = real_part + 1j * imag_part
        padded = jnp.concatenate([spectrum, jnp.zeros_like(spectrum)], axis=-1)
        series = jnp.fft.ifft(padded, axis=-1) * LAGS
        shifted = jnp.fft.fftshift(series, axes=-1)
        return (jnp.real(shifted) * lag_scale).astype(jnp.bfloat16)
    stacked = lax.map(per_block, blocks)
    return stacked.reshape(CHANNELS, SOURCES, LAGS)
```

```python
import math

import jax
import jax.numpy as jnp
from jax import lax
from jax.sharding import PartitionSpec as P

RCV_DIMS = (("x", 16, 4), ("z_hi", 8, 2), ("y", 2, 4), ("core", 1, 2))


def coord(index, stride, size):
    return (index // stride) % size


def shifted(stride, size, step, n):
    pairs = []
    for i in range(n):
        c = (i // stride) % size
        pairs.append((i, i + (((c + step) % size) - c) * stride))
    return pairs


def ring_broadcast(held, me, root, stride, size, n):
    dist = (coord(me, stride, size) - coord(root, stride, size)) % size
    if size == 2:
        got = lax.ppermute(held, "rcv", shifted(stride, size, 1, n))
        return jnp.where(dist == 1, got, held)
    from_below = lax.ppermute(held, "rcv", shifted(stride, size, 1, n))
    from_above = lax.ppermute(held, "rcv", shifted(stride, size, -1, n))
    held = jnp.where(dist == 1, from_below, jnp.where(dist == size - 1, from_above, held))
    for d in range(2, size // 2 + 1):
        got = lax.ppermute(held, "rcv", shifted(stride, size, 1, n))
        held = jnp.where(dist == d, got, held)
    return held


def source_half(spectra, root):
    n = lax.axis_size("rcv")
    me = lax.axis_index("rcv")
    core = me % 2
    partner = lax.ppermute(spectra, "rcv", shifted(1, 2, 1, n))
    held = jnp.where(core == root % 2, spectra, partner)
    halves = held.reshape((2, held.shape[0] // 2) + held.shape[1:])
    half = lax.dynamic_index_in_dim(halves, core, 0, keepdims=False)
    for name, stride, size in RCV_DIMS[:-1]:
        half = ring_broadcast(half, me, root, stride, size, n)
    return half


def cross_terms(receivers, source):
    flipped = jnp.stack([-receivers[:, :, 1], receivers[:, :, 0]], axis=2)
    real_part = jnp.einsum("rwcf,swcf->rsf", receivers, source, preferred_element_type=jnp.float32)
    imag_part = jnp.einsum("rwcf,swcf->rsf", flipped, source, preferred_element_type=jnp.float32)
    return jnp.stack([real_part, imag_part], axis=2)


def lag_table(n_freqs, lag_start, n_lags):
    freq_index = jnp.arange(n_freqs, dtype=jnp.int32)
    lag_index = jnp.arange(n_lags, dtype=jnp.int32) + lag_start
    phase_index = freq_index[:, None] * lag_index[None, :] % (2 * n_freqs)
    angle = math.pi / n_freqs * phase_index.astype(jnp.float32)
    return jnp.concatenate([jnp.cos(angle), -jnp.sin(angle)], axis=0).astype(jnp.bfloat16)


def body(spectra, source_block):
    root = source_block[0]
    win_count = lax.axis_size("win")
    n_freqs = spectra.shape[3]
    all_lags = 2 * n_freqs
    my_lags = all_lags // win_count
    lag_scale = 1.0 / math.sqrt(all_lags * spectra.shape[1] * win_count)
    lag_start = lax.axis_index("win") * my_lags - n_freqs
    table = lag_table(n_freqs, lag_start, my_lags)

    receivers = lax.all_gather(spectra, "win", axis=1, tiled=True)
    half = source_half(spectra, root)
    half = lax.all_gather(half, "win", axis=1, tiled=True)
    other = lax.ppermute(half, "rcv", shifted(1, 2, 1, lax.axis_size("rcv")))
    first = lax.axis_index("rcv") % 2 == 0
    source = jnp.concatenate(
        [jnp.where(first, half, other), jnp.where(first, other, half)], axis=0
    )

    cross_spec = cross_terms(receivers, source).astype(jnp.bfloat16)
    rows, sources = cross_spec.shape[:2]
    flat_spec = cross_spec.reshape(rows * sources, 2 * n_freqs)
    lagged = jnp.dot(flat_spec, table, preferred_element_type=jnp.float32) * lag_scale
    return lagged.astype(jnp.bfloat16).reshape(rows, sources, my_lags)


def solution(mesh):
    in_specs = (P("rcv", "win", None, None), P())
    out_specs = P("rcv", None, "win")
    return jax.shard_map(body, mesh=mesh, in_specs=in_specs, out_specs=out_specs, check_vma=False)
```

```python
import math

import jax
import jax.numpy as jnp
from jax import lax
from jax.sharding import PartitionSpec as P

RCV_DIMS = (("x", 16, 4), ("z_hi", 8, 2), ("y", 2, 4), ("core", 1, 2))


def coord(index, stride, size):
    return (index // stride) % size


def shifted(stride, size, step, n):
    pairs = []
    for i in range(n):
        c = (i // stride) % size
        pairs.append((i, i + (((c + step) % size) - c) * stride))
    return pairs


def ring_broadcast(held, me, root, stride, size, n):
    dist = (coord(me, stride, size) - coord(root, stride, size)) % size
    up = shifted(stride, size, 1, n)
    if size == 2:
        got = lax.ppermute(held, "rcv", up)
        return jnp.where(dist == 1, got, held)
    assert size == 4
    down = shifted(stride, size, -1, n)
    p1, p2 = jnp.split(held, 2, axis=0)
    from_below = lax.ppermute(p1, "rcv", up)
    from_above = lax.ppermute(p2, "rcv", down)
    p1 = jnp.where(dist == 1, from_below, p1)
    p2 = jnp.where(dist == 3, from_above, p2)
    root_here = dist == 0
    from_below = lax.ppermute(jnp.where(root_here, p2, p1), "rcv", up)
    from_above = lax.ppermute(jnp.where(root_here, p1, p2), "rcv", down)
    p1 = jnp.where(dist == 2, from_below, jnp.where(dist == 3, from_above, p1))
    p2 = jnp.where(dist == 1, from_below, jnp.where(dist == 2, from_above, p2))
    return jnp.concatenate([p1, p2], axis=0)


def source_half(block, root):
    n = lax.axis_size("rcv")
    me = lax.axis_index("rcv")
    core = me % 2
    partner = lax.ppermute(block, "rcv", shifted(1, 2, 1, n))
    held = jnp.where(core == root % 2, block, partner)
    halves = held.reshape((2, held.shape[0] // 2) + held.shape[1:])
    half = lax.dynamic_index_in_dim(halves, core, 0, keepdims=False)
    for name, stride, size in RCV_DIMS[:-1]:
        half = ring_broadcast(half, me, root, stride, size, n)
    return half


def lag_table(n_freqs, lag_start, n_lags):
    freq_index = jnp.arange(n_freqs, dtype=jnp.int32)
    lag_index = jnp.arange(n_lags, dtype=jnp.int32) + lag_start
    phase_index = freq_index[:, None] * lag_index[None, :] % (2 * n_freqs)
    angle = math.pi / n_freqs * phase_index.astype(jnp.float32)
    return jnp.cos(angle).astype(jnp.bfloat16), (-jnp.sin(angle)).astype(jnp.bfloat16)


def body(spectra, source_block):
    root = source_block[0]
    win_count = lax.axis_size("win")
    n = lax.axis_size("rcv")
    n_freqs = spectra.shape[3]
    all_lags = 2 * n_freqs
    my_lags = all_lags // win_count
    lag_scale = 1.0 / math.sqrt(all_lags * spectra.shape[1] * win_count)
    lag_start = lax.axis_index("win") * my_lags - n_freqs
    table = lax.optimization_barrier(lag_table(n_freqs, lag_start, my_lags))

    block = spectra.transpose(3, 1, 2, 0)
    receivers = lax.all_gather(block, "win", axis=1, tiled=True)
    half = source_half(block, root)
    half, receivers = lax.optimization_barrier((half, receivers))
    half = lax.all_gather(half, "win", axis=1, tiled=True)
    other = lax.ppermute(half, "rcv", shifted(1, 2, 1, n))
    first = lax.axis_index("rcv") % 2 == 0
    source = jnp.concatenate(
        [jnp.where(first, half, other), jnp.where(first, other, half)], axis=0
    )

    freqs, windows, two, rows = receivers.shape
    flipped = jnp.stack([source[:, :, 1], -source[:, :, 0]], axis=2)
    terms_r = receivers.reshape(freqs, windows * two, rows)
    real_part = jnp.einsum(
        "fkr,fks->frs", terms_r, source.reshape(freqs, windows * two, -1),
        preferred_element_type=jnp.float32,
    ).astype(jnp.bfloat16)
    imag_part = jnp.einsum(
        "fkr,fks->frs", terms_r, flipped.reshape(freqs, windows * two, -1),
        preferred_element_type=jnp.float32,
    ).astype(jnp.bfloat16)
    cos_t, sin_t = table
    lagged = jnp.einsum("fl,frs->lrs", cos_t, real_part, preferred_element_type=jnp.float32)
    lagged = lagged + jnp.einsum("fl,frs->lrs", sin_t, imag_part, preferred_element_type=jnp.float32)
    return (lagged * lag_scale).astype(jnp.bfloat16).transpose(1, 2, 0)


def solution(mesh):
    in_specs = (P("rcv", "win", None, None), P())
    out_specs = P("rcv", None, "win")
    return jax.shard_map(body, mesh=mesh, in_specs=in_specs, out_specs=out_specs, check_vma=False)
```

```python
import math

import jax
import jax.numpy as jnp
from jax import lax
from jax.experimental.layout import Layout, with_layout_constraint
from jax.sharding import PartitionSpec as P

RCV_DIMS = (("x", 16, 4), ("z_hi", 8, 2), ("y", 2, 4), ("core", 1, 2))


def coord(index, stride, size):
    return (index // stride) % size


def shifted(stride, size, step, n):
    pairs = []
    for i in range(n):
        c = (i // stride) % size
        pairs.append((i, i + (((c + step) % size) - c) * stride))
    return pairs


def ring_broadcast(held, me, root, stride, size, n):
    dist = (coord(me, stride, size) - coord(root, stride, size)) % size
    up = shifted(stride, size, 1, n)
    if size == 2:
        got = lax.ppermute(held, "rcv", up)
        return jnp.where(dist == 1, got, held)
    assert size == 4
    down = shifted(stride, size, -1, n)
    p1, p2 = jnp.split(held, 2, axis=0)
    from_below = lax.ppermute(p1, "rcv", up)
    from_above = lax.ppermute(p2, "rcv", down)
    p1 = jnp.where(dist == 1, from_below, p1)
    p2 = jnp.where(dist == 3, from_above, p2)
    root_here = dist == 0
    from_below = lax.ppermute(jnp.where(root_here, p2, p1), "rcv", up)
    from_above = lax.ppermute(jnp.where(root_here, p1, p2), "rcv", down)
    p1 = jnp.where(dist == 2, from_below, jnp.where(dist == 3, from_above, p1))
    p2 = jnp.where(dist == 1, from_below, jnp.where(dist == 2, from_above, p2))
    return jnp.concatenate([p1, p2], axis=0)


def source_half(block, root):
    n = lax.axis_size("rcv")
    me = lax.axis_index("rcv")
    core = me % 2
    partner = lax.ppermute(block, "rcv", shifted(1, 2, 1, n))
    held = jnp.where(core == root % 2, block, partner)
    halves = held.reshape((2, held.shape[0] // 2) + held.shape[1:])
    half = lax.dynamic_index_in_dim(halves, core, 0, keepdims=False)
    for name, stride, size in RCV_DIMS[:-1]:
        half = ring_broadcast(half, me, root, stride, size, n)
    return half


def lag_table(n_freqs, lag_start, n_lags):
    freq_index = jnp.arange(n_freqs, dtype=jnp.int32)
    lag_index = jnp.arange(n_lags, dtype=jnp.int32) + lag_start
    phase_index = lag_index[:, None] * freq_index[None, :] % (2 * n_freqs)
    angle = math.pi / n_freqs * phase_index.astype(jnp.float32)
    return jnp.cos(angle).astype(jnp.bfloat16), (-jnp.sin(angle)).astype(jnp.bfloat16)


def body(spectra, source_block):
    root = source_block[0]
    win_count = lax.axis_size("win")
    n = lax.axis_size("rcv")
    n_freqs = spectra.shape[3]
    all_lags = 2 * n_freqs
    my_lags = all_lags // win_count
    lag_scale = 1.0 / math.sqrt(all_lags * spectra.shape[1] * win_count)
    lag_start = lax.axis_index("win") * my_lags - n_freqs
    table = lax.optimization_barrier(lag_table(n_freqs, lag_start, my_lags))

    block = with_layout_constraint(spectra.transpose(3, 1, 2, 0), Layout((0, 1, 2, 3)))
    receivers = lax.all_gather(block, "win", axis=1, tiled=True)
    half = source_half(block, root)
    half, receivers = lax.optimization_barrier((half, receivers))
    half = lax.all_gather(half, "win", axis=1, tiled=True)
    other = lax.ppermute(half, "rcv", shifted(1, 2, 1, n))
    first = lax.axis_index("rcv") % 2 == 0
    source = jnp.concatenate(
        [jnp.where(first, half, other), jnp.where(first, other, half)], axis=0
    )

    freqs, windows, two, rows = receivers.shape
    flipped = jnp.stack([source[:, :, 1], -source[:, :, 0]], axis=2)
    as_read = Layout((0, 1, 2, 3))
    source, flipped = with_layout_constraint((source, flipped), (as_read, as_read))
    terms_r = receivers.reshape(freqs, windows * two, rows)
    real_part = jnp.einsum(
        "fkr,fks->frs", terms_r, source.reshape(freqs, windows * two, -1),
        preferred_element_type=jnp.float32,
    ).astype(jnp.bfloat16)
    imag_part = jnp.einsum(
        "fkr,fks->frs", terms_r, flipped.reshape(freqs, windows * two, -1),
        preferred_element_type=jnp.float32,
    ).astype(jnp.bfloat16)
    real_part, imag_part = with_layout_constraint(
        (real_part, imag_part), (Layout((0, 1, 2)), Layout((0, 1, 2)))
    )
    cos_t, sin_t = table
    lagged = jnp.einsum("lf,frs->lrs", cos_t, real_part, preferred_element_type=jnp.float32)
    lagged = lagged + jnp.einsum("lf,frs->lrs", sin_t, imag_part, preferred_element_type=jnp.float32)
    lagged = with_layout_constraint(lagged, Layout((1, 2, 0)))
    return (lagged * lag_scale).astype(jnp.bfloat16).transpose(1, 2, 0)


def solution(mesh):
    in_specs = (P("rcv", "win", None, None), P())
    out_specs = P("rcv", None, "win")
    return jax.shard_map(body, mesh=mesh, in_specs=in_specs, out_specs=out_specs, check_vma=False)
```

```python
import math

import jax
import jax.numpy as jnp
from jax import lax
from jax.experimental.layout import Layout, with_layout_constraint
from jax.sharding import PartitionSpec as P

RCV_DIMS = (("x", 16, 4), ("z_hi", 8, 2), ("y", 2, 4), ("core", 1, 2))


def coord(index, stride, size):
    return (index // stride) % size


def shifted(stride, size, step, n):
    pairs = []
    for i in range(n):
        c = (i // stride) % size
        pairs.append((i, i + (((c + step) % size) - c) * stride))
    return pairs


def ring_broadcast(held, me, root, stride, size, n):
    dist = (coord(me, stride, size) - coord(root, stride, size)) % size
    up = shifted(stride, size, 1, n)
    if size == 2:
        got = lax.ppermute(held, "rcv", up)
        return jnp.where(dist == 1, got, held)
    assert size == 4
    down = shifted(stride, size, -1, n)
    p1, p2 = jnp.split(held, 2, axis=0)
    from_below = lax.ppermute(p1, "rcv", up)
    from_above = lax.ppermute(p2, "rcv", down)
    p1 = jnp.where(dist == 1, from_below, p1)
    p2 = jnp.where(dist == 3, from_above, p2)
    root_here = dist == 0
    from_below = lax.ppermute(jnp.where(root_here, p2, p1), "rcv", up)
    from_above = lax.ppermute(jnp.where(root_here, p1, p2), "rcv", down)
    p1 = jnp.where(dist == 2, from_below, jnp.where(dist == 3, from_above, p1))
    p2 = jnp.where(dist == 1, from_below, jnp.where(dist == 2, from_above, p2))
    return jnp.concatenate([p1, p2], axis=0)


def source_half(block, root):
    n = lax.axis_size("rcv")
    me = lax.axis_index("rcv")
    core = me % 2
    partner = lax.ppermute(block, "rcv", shifted(1, 2, 1, n))
    held = jnp.where(core == root % 2, block, partner)
    halves = held.reshape((2, held.shape[0] // 2) + held.shape[1:])
    half = lax.dynamic_index_in_dim(halves, core, 0, keepdims=False)
    for name, stride, size in RCV_DIMS[:-1]:
        half = ring_broadcast(half, me, root, stride, size, n)
    return half


def lag_table(n_freqs, lag_start, n_lags):
    freq_index = jnp.arange(n_freqs, dtype=jnp.int32)
    lag_index = jnp.arange(n_lags, dtype=jnp.int32) + lag_start
    phase_index = lag_index[:, None] * freq_index[None, :] % (2 * n_freqs)
    angle = math.pi / n_freqs * phase_index.astype(jnp.float32)
    return jnp.cos(angle).astype(jnp.bfloat16), (-jnp.sin(angle)).astype(jnp.bfloat16)


def body(spectra, source_block):
    root = source_block[0]
    win_count = lax.axis_size("win")
    n = lax.axis_size("rcv")
    n_freqs = spectra.shape[3]
    all_lags = 2 * n_freqs
    my_lags = all_lags // win_count
    lag_scale = 1.0 / math.sqrt(all_lags * spectra.shape[1] * win_count)
    lag_start = lax.axis_index("win") * my_lags - n_freqs
    table = lax.optimization_barrier(lag_table(n_freqs, lag_start, my_lags))

    receivers = lax.all_gather(spectra, "win", axis=1, tiled=True)
    half = source_half(spectra, root)
    half, receivers = lax.optimization_barrier((half, receivers))
    half = lax.all_gather(half, "win", axis=1, tiled=True)
    other = lax.ppermute(half, "rcv", shifted(1, 2, 1, n))
    first = lax.axis_index("rcv") % 2 == 0
    source = jnp.concatenate(
        [jnp.where(first, half, other), jnp.where(first, other, half)], axis=0
    )

    rows, windows, two, freqs = receivers.shape
    flipped = jnp.stack([source[:, :, 1], -source[:, :, 0]], axis=2)
    terms_r = receivers.reshape(rows, windows * two, freqs)
    real_part = jnp.einsum(
        "rkf,skf->frs", terms_r, source.reshape(-1, windows * two, freqs),
        preferred_element_type=jnp.float32,
    ).astype(jnp.bfloat16)
    imag_part = jnp.einsum(
        "rkf,skf->frs", terms_r, flipped.reshape(-1, windows * two, freqs),
        preferred_element_type=jnp.float32,
    ).astype(jnp.bfloat16)
    real_part, imag_part = with_layout_constraint(
        (real_part, imag_part), (Layout((0, 1, 2)), Layout((0, 1, 2)))
    )
    cos_t, sin_t = table
    lagged = jnp.einsum("lf,frs->lrs", cos_t, real_part, preferred_element_type=jnp.float32)
    lagged = lagged + jnp.einsum("lf,frs->lrs", sin_t, imag_part, preferred_element_type=jnp.float32)
    lagged = with_layout_constraint(lagged, Layout((1, 2, 0)))
    return (lagged * lag_scale).astype(jnp.bfloat16).transpose(1, 2, 0)


def solution(mesh):
    in_specs = (P("rcv", "win", None, None), P())
    out_specs = P("rcv", None, "win")
    return jax.shard_map(body, mesh=mesh, in_specs=in_specs, out_specs=out_specs, check_vma=False)
```

```python
import math

import jax
import jax.numpy as jnp
from jax import lax
from jax.experimental.layout import Layout, with_layout_constraint
from jax.sharding import PartitionSpec as P

RCV_DIMS = (("x", 16, 4), ("z_hi", 8, 2), ("y", 2, 4), ("core", 1, 2))


def coord(index, stride, size):
    return (index // stride) % size


def shifted(stride, size, step, n):
    pairs = []
    for i in range(n):
        c = (i // stride) % size
        pairs.append((i, i + (((c + step) % size) - c) * stride))
    return pairs


def ring_broadcast(held, me, root, stride, size, n):
    dist = (coord(me, stride, size) - coord(root, stride, size)) % size
    up = shifted(stride, size, 1, n)
    if size == 2:
        got = lax.ppermute(held, "rcv", up)
        return jnp.where(dist == 1, got, held)
    assert size == 4
    down = shifted(stride, size, -1, n)
    p1, p2 = jnp.split(held, 2, axis=1)
    from_below = lax.ppermute(p1, "rcv", up)
    from_above = lax.ppermute(p2, "rcv", down)
    p1 = jnp.where(dist == 1, from_below, p1)
    p2 = jnp.where(dist == 3, from_above, p2)
    root_here = dist == 0
    from_below = lax.ppermute(jnp.where(root_here, p2, p1), "rcv", up)
    from_above = lax.ppermute(jnp.where(root_here, p1, p2), "rcv", down)
    p1 = jnp.where(dist == 2, from_below, jnp.where(dist == 3, from_above, p1))
    p2 = jnp.where(dist == 1, from_below, jnp.where(dist == 2, from_above, p2))
    return jnp.concatenate([p1, p2], axis=1)


def source_half(block, root):
    n = lax.axis_size("rcv")
    me = lax.axis_index("rcv")
    core = me % 2
    partner = lax.ppermute(block, "rcv", shifted(1, 2, 1, n))
    held = jnp.where(core == root % 2, block, partner)
    halves = held.reshape(held.shape[:1] + (2, held.shape[1] // 2) + held.shape[2:])
    half = lax.dynamic_index_in_dim(halves, core, 1, keepdims=False)
    for name, stride, size in RCV_DIMS[:-1]:
        half = ring_broadcast(half, me, root, stride, size, n)
    return half


def lag_table(n_freqs, lag_start, n_lags):
    freq_index = jnp.arange(n_freqs, dtype=jnp.int32)
    lag_index = jnp.arange(n_lags, dtype=jnp.int32) + lag_start
    phase_index = lag_index[:, None] * freq_index[None, :] % (2 * n_freqs)
    angle = math.pi / n_freqs * phase_index.astype(jnp.float32)
    return jnp.cos(angle).astype(jnp.bfloat16), (-jnp.sin(angle)).astype(jnp.bfloat16)


def body(spectra, source_block):
    root = source_block[0]
    win_count = lax.axis_size("win")
    n = lax.axis_size("rcv")
    n_freqs = spectra.shape[3]
    all_lags = 2 * n_freqs
    my_lags = all_lags // win_count
    lag_scale = 1.0 / math.sqrt(all_lags * spectra.shape[1] * win_count)
    lag_start = lax.axis_index("win") * my_lags - n_freqs
    table = lax.optimization_barrier(lag_table(n_freqs, lag_start, my_lags))

    block = with_layout_constraint(spectra.transpose(1, 3, 2, 0), Layout((0, 1, 2, 3)))
    receivers = lax.all_gather(block, "win", axis=0, tiled=True)
    half = source_half(block, root)
    half, receivers = lax.optimization_barrier((half, receivers))
    half = lax.all_gather(half, "win", axis=0, tiled=True)
    other = lax.ppermute(half, "rcv", shifted(1, 2, 1, n))
    first = lax.axis_index("rcv") % 2 == 0
    source = jnp.concatenate(
        [jnp.where(first, half, other), jnp.where(first, other, half)], axis=1
    )

    flipped = jnp.stack([source[:, :, 1], -source[:, :, 0]], axis=2)
    real_part = jnp.einsum(
        "wfcr,wfcs->frs", receivers, source, preferred_element_type=jnp.float32
    ).astype(jnp.bfloat16)
    imag_part = jnp.einsum(
        "wfcr,wfcs->frs", receivers, flipped, preferred_element_type=jnp.float32
    ).astype(jnp.bfloat16)
    real_part, imag_part = with_layout_constraint(
        (real_part, imag_part), (Layout((0, 1, 2)), Layout((0, 1, 2)))
    )
    cos_t, sin_t = table
    lagged = jnp.einsum("lf,frs->lrs", cos_t, real_part, preferred_element_type=jnp.float32)
    lagged = lagged + jnp.einsum("lf,frs->lrs", sin_t, imag_part, preferred_element_type=jnp.float32)
    lagged = with_layout_constraint(lagged, Layout((1, 2, 0)))
    return (lagged * lag_scale).astype(jnp.bfloat16).transpose(1, 2, 0)


def solution(mesh):
    in_specs = (P("rcv", "win", None, None), P())
    out_specs = P("rcv", None, "win")
    return jax.shard_map(body, mesh=mesh, in_specs=in_specs, out_specs=out_specs, check_vma=False)
```

```python
import math

import jax
import jax.numpy as jnp
from jax import lax
from jax.experimental.layout import Layout, with_layout_constraint
from jax.sharding import PartitionSpec as P

RCV_DIMS = (("x", 16, 4), ("z_hi", 8, 2), ("y", 2, 4), ("core", 1, 2))


def coord(index, stride, size):
    return (index // stride) % size


def shifted(stride, size, step, n):
    pairs = []
    for i in range(n):
        c = (i // stride) % size
        pairs.append((i, i + (((c + step) % size) - c) * stride))
    return pairs


def ring_broadcast(held, me, root, stride, size, n):
    dist = (coord(me, stride, size) - coord(root, stride, size)) % size
    up = shifted(stride, size, 1, n)
    if size == 2:
        got = lax.ppermute(held, "rcv", up)
        return jnp.where(dist == 1, got, held)
    assert size == 4
    down = shifted(stride, size, -1, n)
    p1, p2 = jnp.split(held, 2, axis=1)
    from_below = lax.ppermute(p1, "rcv", up)
    from_above = lax.ppermute(p2, "rcv", down)
    p1 = jnp.where(dist == 1, from_below, p1)
    p2 = jnp.where(dist == 3, from_above, p2)
    root_here = dist == 0
    from_below = lax.ppermute(jnp.where(root_here, p2, p1), "rcv", up)
    from_above = lax.ppermute(jnp.where(root_here, p1, p2), "rcv", down)
    p1 = jnp.where(dist == 2, from_below, jnp.where(dist == 3, from_above, p1))
    p2 = jnp.where(dist == 1, from_below, jnp.where(dist == 2, from_above, p2))
    return jnp.concatenate([p1, p2], axis=1)


def source_half(block, root):
    n = lax.axis_size("rcv")
    me = lax.axis_index("rcv")
    core = me % 2
    partner = lax.ppermute(block, "rcv", shifted(1, 2, 1, n))
    held = jnp.where(core == root % 2, block, partner)
    halves = held.reshape(held.shape[:1] + (2, held.shape[1] // 2) + held.shape[2:])
    half = lax.dynamic_index_in_dim(halves, core, 1, keepdims=False)
    for name, stride, size in RCV_DIMS[:-1]:
        half = ring_broadcast(half, me, root, stride, size, n)
    return half


def line_gather(block, axis):
    n = lax.axis_size(axis)
    k = lax.axis_index(axis)
    up = [(i, i + 1) for i in range(n - 1)]
    down = [(i + 1, i) for i in range(n - 1)]
    below, above = [block], [block]
    for _ in range(n - 1):
        below.append(lax.ppermute(below[-1], axis, up))
        above.append(lax.ppermute(above[-1], axis, down))
    slots = []
    for origin in range(n):
        slot = block
        for d in range(1, n):
            slot = jnp.where(k - d == origin, below[d], slot)
            slot = jnp.where(k + d == origin, above[d], slot)
        slots.append(slot)
    return jnp.concatenate(slots, axis=0)


def lag_table(n_freqs, lag_start, n_lags):
    freq_index = jnp.arange(n_freqs, dtype=jnp.int32)
    lag_index = jnp.arange(n_lags, dtype=jnp.int32) + lag_start
    phase_index = lag_index[:, None] * freq_index[None, :] % (2 * n_freqs)
    angle = math.pi / n_freqs * phase_index.astype(jnp.float32)
    return jnp.cos(angle).astype(jnp.bfloat16), (-jnp.sin(angle)).astype(jnp.bfloat16)


def body(spectra, source_block):
    root = source_block[0]
    win_count = lax.axis_size("win")
    n = lax.axis_size("rcv")
    n_freqs = spectra.shape[3]
    all_lags = 2 * n_freqs
    my_lags = all_lags // win_count
    lag_scale = 1.0 / math.sqrt(all_lags * spectra.shape[1] * win_count)
    lag_start = lax.axis_index("win") * my_lags - n_freqs
    table = lax.optimization_barrier(lag_table(n_freqs, lag_start, my_lags))

    block = with_layout_constraint(spectra.transpose(1, 3, 2, 0), Layout((0, 1, 2, 3)))
    receivers = lax.all_gather(block, "win", axis=0, tiled=True)
    half = source_half(block, root)
    half = line_gather(half, "win")
    other = lax.ppermute(half, "rcv", shifted(1, 2, 1, n))
    first = lax.axis_index("rcv") % 2 == 0
    source = jnp.concatenate(
        [jnp.where(first, half, other), jnp.where(first, other, half)], axis=1
    )

    flipped = jnp.stack([source[:, :, 1], -source[:, :, 0]], axis=2)
    real_part = jnp.einsum(
        "wfcr,wfcs->frs", receivers, source, preferred_element_type=jnp.float32
    ).astype(jnp.bfloat16)
    imag_part = jnp.einsum(
        "wfcr,wfcs->frs", receivers, flipped, preferred_element_type=jnp.float32
    ).astype(jnp.bfloat16)
    real_part, imag_part = with_layout_constraint(
        (real_part, imag_part), (Layout((0, 1, 2)), Layout((0, 1, 2)))
    )
    cos_t, sin_t = table
    lagged = jnp.einsum("lf,frs->lrs", cos_t, real_part, preferred_element_type=jnp.float32)
    lagged = lagged + jnp.einsum("lf,frs->lrs", sin_t, imag_part, preferred_element_type=jnp.float32)
    lagged = with_layout_constraint(lagged, Layout((1, 2, 0)))
    return (lagged * lag_scale).astype(jnp.bfloat16).transpose(1, 2, 0)


def solution(mesh):
    in_specs = (P("rcv", "win", None, None), P())
    out_specs = P("rcv", None, "win")
    return jax.shard_map(body, mesh=mesh, in_specs=in_specs, out_specs=out_specs, check_vma=False)
```

```python
import math

import jax
import jax.numpy as jnp
from jax import lax
from jax.experimental.layout import Layout, with_layout_constraint
from jax.sharding import PartitionSpec as P

RCV_DIMS = (("x", 16, 4), ("z_hi", 8, 2), ("y", 2, 4), ("core", 1, 2))


def coord(index, stride, size):
    return (index // stride) % size


def shifted(stride, size, step, n):
    pairs = []
    for i in range(n):
        c = (i // stride) % size
        pairs.append((i, i + (((c + step) % size) - c) * stride))
    return pairs


def ring_broadcast(held, me, root, stride, size, n):
    dist = (coord(me, stride, size) - coord(root, stride, size)) % size
    up = shifted(stride, size, 1, n)
    if size == 2:
        sides = [
            [(i, i + stride) for i in range(n) if coord(i, stride, size) == 0],
            [(i, i - stride) for i in range(n) if coord(i, stride, size) == 1],
        ]
        got = lax.switch(
            coord(root, stride, size),
            [lambda h, pairs=pairs: lax.ppermute(h, "rcv", pairs) for pairs in sides],
            held,
        )
        return jnp.where(dist == 1, got, held)
    assert size == 4
    down = shifted(stride, size, -1, n)
    p1, p2 = jnp.split(held, 2, axis=1)
    from_below = lax.ppermute(p1, "rcv", up)
    from_above = lax.ppermute(p2, "rcv", down)
    p1 = jnp.where(dist == 1, from_below, p1)
    p2 = jnp.where(dist == 3, from_above, p2)
    root_here = dist == 0
    from_below = lax.ppermute(jnp.where(root_here, p2, p1), "rcv", up)
    from_above = lax.ppermute(jnp.where(root_here, p1, p2), "rcv", down)
    p1 = jnp.where(dist == 2, from_below, jnp.where(dist == 3, from_above, p1))
    p2 = jnp.where(dist == 1, from_below, jnp.where(dist == 2, from_above, p2))
    return jnp.concatenate([p1, p2], axis=1)


def source_half(block, root):
    n = lax.axis_size("rcv")
    me = lax.axis_index("rcv")
    core = me % 2
    partner = lax.ppermute(block, "rcv", shifted(1, 2, 1, n))
    held = jnp.where(core == root % 2, block, partner)
    halves = held.reshape(held.shape[:1] + (2, held.shape[1] // 2) + held.shape[2:])
    half = lax.dynamic_index_in_dim(halves, core, 1, keepdims=False)
    for name, stride, size in RCV_DIMS[:-1]:
        half = ring_broadcast(half, me, root, stride, size, n)
    return half


def lag_table(n_freqs, lag_start, n_lags):
    freq_index = jnp.arange(n_freqs, dtype=jnp.int32)
    lag_index = jnp.arange(n_lags, dtype=jnp.int32) + lag_start
    phase_index = lag_index[:, None] * freq_index[None, :] % (2 * n_freqs)
    angle = math.pi / n_freqs * phase_index.astype(jnp.float32)
    return jnp.cos(angle).astype(jnp.bfloat16), (-jnp.sin(angle)).astype(jnp.bfloat16)


def body(spectra, source_block):
    root = source_block[0]
    win_count = lax.axis_size("win")
    n = lax.axis_size("rcv")
    n_freqs = spectra.shape[3]
    all_lags = 2 * n_freqs
    my_lags = all_lags // win_count
    lag_scale = 1.0 / math.sqrt(all_lags * spectra.shape[1] * win_count)
    lag_start = lax.axis_index("win") * my_lags - n_freqs
    table = lax.optimization_barrier(lag_table(n_freqs, lag_start, my_lags))

    block = with_layout_constraint(spectra.transpose(1, 3, 2, 0), Layout((0, 1, 2, 3)))
    receivers = lax.all_gather(block, "win", axis=0, tiled=True)
    half = source_half(block, root)
    half, receivers, table = lax.optimization_barrier((half, receivers, table))
    half = lax.all_gather(half, "win", axis=0, tiled=True)
    other = lax.ppermute(half, "rcv", shifted(1, 2, 1, n))
    first = lax.axis_index("rcv") % 2 == 0
    source = jnp.concatenate(
        [jnp.where(first, half, other), jnp.where(first, other, half)], axis=1
    )

    flipped = jnp.stack([source[:, :, 1], -source[:, :, 0]], axis=2)
    real_part = jnp.einsum(
        "wfcr,wfcs->frs", receivers, source, preferred_element_type=jnp.float32
    ).astype(jnp.bfloat16)
    imag_part = jnp.einsum(
        "wfcr,wfcs->frs", receivers, flipped, preferred_element_type=jnp.float32
    ).astype(jnp.bfloat16)
    real_part, imag_part = with_layout_constraint(
        (real_part, imag_part), (Layout((0, 1, 2)), Layout((0, 1, 2)))
    )
    cos_t, sin_t = table
    lagged = jnp.einsum("lf,frs->lrs", cos_t, real_part, preferred_element_type=jnp.float32)
    lagged = lagged + jnp.einsum("lf,frs->lrs", sin_t, imag_part, preferred_element_type=jnp.float32)
    lagged = with_layout_constraint(lagged, Layout((1, 2, 0)))
    return (lagged * lag_scale).astype(jnp.bfloat16).transpose(1, 2, 0)


def solution(mesh):
    in_specs = (P("rcv", "win", None, None), P())
    out_specs = P("rcv", None, "win")
    return jax.shard_map(body, mesh=mesh, in_specs=in_specs, out_specs=out_specs, check_vma=False)
```

```python
import math

import jax
import jax.numpy as jnp
from jax import lax
from jax.experimental.layout import Layout, with_layout_constraint
from jax.sharding import PartitionSpec as P

RCV_DIMS = (("x", 16, 4), ("z_hi", 8, 2), ("y", 2, 4), ("core", 1, 2))


def coord(index, stride, size):
    return (index // stride) % size


def shifted(stride, size, step, n):
    pairs = []
    for i in range(n):
        c = (i // stride) % size
        pairs.append((i, i + (((c + step) % size) - c) * stride))
    return pairs


def ring_broadcast(held, me, root, stride, size, n):
    dist = (coord(me, stride, size) - coord(root, stride, size)) % size
    up = shifted(stride, size, 1, n)
    if size == 2:
        got = lax.ppermute(held, "rcv", up)
        return jnp.where(dist == 1, got, held)
    assert size == 4
    down = shifted(stride, size, -1, n)
    p1, p2 = jnp.split(held, 2, axis=1)
    from_below = lax.ppermute(p1, "rcv", up)
    from_above = lax.ppermute(p2, "rcv", down)
    p1 = jnp.where(dist == 1, from_below, p1)
    p2 = jnp.where(dist == 3, from_above, p2)
    root_here = dist == 0
    from_below = lax.ppermute(jnp.where(root_here, p2, p1), "rcv", up)
    from_above = lax.ppermute(jnp.where(root_here, p1, p2), "rcv", down)
    p1 = jnp.where(dist == 2, from_below, jnp.where(dist == 3, from_above, p1))
    p2 = jnp.where(dist == 1, from_below, jnp.where(dist == 2, from_above, p2))
    return jnp.concatenate([p1, p2], axis=1)


def source_half(block, root):
    n = lax.axis_size("rcv")
    me = lax.axis_index("rcv")
    core = me % 2
    partner = lax.ppermute(block, "rcv", shifted(1, 2, 1, n))
    held = jnp.where(core == root % 2, block, partner)
    halves = held.reshape(held.shape[:1] + (2, held.shape[1] // 2) + held.shape[2:])
    half = lax.dynamic_index_in_dim(halves, core, 1, keepdims=False)
    for name, stride, size in RCV_DIMS[:-1]:
        half = ring_broadcast(half, me, root, stride, size, n)
    return half


def lag_table(n_freqs, lag_start, n_lags):
    freq_index = jnp.arange(n_freqs, dtype=jnp.int32)
    lag_index = jnp.arange(n_lags, dtype=jnp.int32) + lag_start
    phase_index = lag_index[:, None] * freq_index[None, :] % (2 * n_freqs)
    angle = math.pi / n_freqs * phase_index.astype(jnp.float32)
    return jnp.cos(angle).astype(jnp.bfloat16), (-jnp.sin(angle)).astype(jnp.bfloat16)


def body(spectra, source_block):
    root = source_block[0]
    win_count = lax.axis_size("win")
    n = lax.axis_size("rcv")
    n_freqs = spectra.shape[3]
    all_lags = 2 * n_freqs
    my_lags = all_lags // win_count
    lag_scale = 1.0 / math.sqrt(all_lags * spectra.shape[1] * win_count)
    lag_start = lax.axis_index("win") * my_lags - n_freqs
    table = lax.optimization_barrier(lag_table(n_freqs, lag_start, my_lags))

    block = with_layout_constraint(spectra.transpose(1, 3, 2, 0), Layout((0, 1, 2, 3)))
    receivers = lax.all_gather(block, "win", axis=0, tiled=True)
    half = source_half(block, root)
    half, receivers, table = lax.optimization_barrier((half, receivers, table))
    half = lax.all_gather(half, "win", axis=0, tiled=True)
    other = lax.ppermute(half, "rcv", shifted(1, 2, 1, n))
    first = lax.axis_index("rcv") % 2 == 0
    source = jnp.concatenate(
        [jnp.where(first, half, other), jnp.where(first, other, half)], axis=1
    )

    flipped = jnp.stack([source[:, :, 1], -source[:, :, 0]], axis=2)
    real_part = jnp.einsum(
        "wfcr,wfcs->frs", receivers, source, preferred_element_type=jnp.float32
    ).astype(jnp.bfloat16)
    imag_part = jnp.einsum(
        "wfcr,wfcs->frs", receivers, flipped, preferred_element_type=jnp.float32
    ).astype(jnp.bfloat16)
    real_part, imag_part = with_layout_constraint(
        (real_part, imag_part), (Layout((0, 1, 2)), Layout((0, 1, 2)))
    )
    cos_t, sin_t = table
    lagged = jnp.einsum("lf,frs->lrs", cos_t, real_part, preferred_element_type=jnp.float32)
    lagged = lagged + jnp.einsum("lf,frs->lrs", sin_t, imag_part, preferred_element_type=jnp.float32)
    lagged = with_layout_constraint(lagged, Layout((1, 2, 0)))
    return (lagged * lag_scale).astype(jnp.bfloat16).transpose(1, 2, 0)


def solution(mesh):
    in_specs = (P("rcv", "win", None, None), P())
    out_specs = P("rcv", None, "win")
    return jax.shard_map(body, mesh=mesh, in_specs=in_specs, out_specs=out_specs, check_vma=False)
```

```python
import math

import jax
import jax.numpy as jnp
from jax import lax
from jax.experimental.layout import Layout, with_layout_constraint
from jax.sharding import PartitionSpec as P

RCV_DIMS = (("x", 16, 4), ("z_hi", 8, 2), ("y", 2, 4), ("core", 1, 2))


def coord(index, stride, size):
    return (index // stride) % size


def shifted(stride, size, step, n):
    pairs = []
    for i in range(n):
        c = (i // stride) % size
        pairs.append((i, i + (((c + step) % size) - c) * stride))
    return pairs


def ring_broadcast(held, me, root, stride, size, n):
    dist = (coord(me, stride, size) - coord(root, stride, size)) % size
    up = shifted(stride, size, 1, n)
    if size == 2:
        got = lax.ppermute(held, "rcv", up)
        return jnp.where(dist == 1, got, held)
    assert size == 4
    down = shifted(stride, size, -1, n)
    p1, p2 = jnp.split(held, 2, axis=1)
    from_below = lax.ppermute(p1, "rcv", up)
    from_above = lax.ppermute(p2, "rcv", down)
    p1 = jnp.where(dist == 1, from_below, p1)
    p2 = jnp.where(dist == 3, from_above, p2)
    root_here = dist == 0
    from_below = lax.ppermute(jnp.where(root_here, p2, p1), "rcv", up)
    from_above = lax.ppermute(jnp.where(root_here, p1, p2), "rcv", down)
    p1 = jnp.where(dist == 2, from_below, jnp.where(dist == 3, from_above, p1))
    p2 = jnp.where(dist == 1, from_below, jnp.where(dist == 2, from_above, p2))
    return jnp.concatenate([p1, p2], axis=1)


def source_half(block, root):
    n = lax.axis_size("rcv")
    me = lax.axis_index("rcv")
    core = me % 2
    partner = lax.ppermute(block, "rcv", shifted(1, 2, 1, n))
    held = jnp.where(core == root % 2, block, partner)
    halves = held.reshape(held.shape[:1] + (2, held.shape[1] // 2) + held.shape[2:])
    half = lax.dynamic_index_in_dim(halves, core, 1, keepdims=False)
    for name, stride, size in RCV_DIMS[:-1]:
        half = ring_broadcast(half, me, root, stride, size, n)
    return half


def lag_table(n_freqs, lag_start, n_lags):
    freq_index = jnp.arange(n_freqs, dtype=jnp.int32)
    lag_index = jnp.arange(n_lags, dtype=jnp.int32) + lag_start
    phase_index = lag_index[:, None] * freq_index[None, :] % (2 * n_freqs)
    angle = math.pi / n_freqs * phase_index.astype(jnp.float32)
    return jnp.cos(angle).astype(jnp.bfloat16), (-jnp.sin(angle)).astype(jnp.bfloat16)


def body(spectra, source_block):
    root = source_block[0]
    win_count = lax.axis_size("win")
    n = lax.axis_size("rcv")
    n_freqs = spectra.shape[3]
    all_lags = 2 * n_freqs
    my_lags = all_lags // win_count
    lag_scale = 1.0 / math.sqrt(all_lags * spectra.shape[1] * win_count)
    lag_start = lax.axis_index("win") * my_lags - n_freqs
    table = lax.optimization_barrier(lag_table(n_freqs, lag_start, my_lags))

    block = with_layout_constraint(spectra.transpose(1, 3, 2, 0), Layout((0, 1, 2, 3)))
    receivers = lax.all_gather(block, "win", axis=0, tiled=True)
    half = source_half(block, root)
    half, receivers, table = lax.optimization_barrier((half, receivers, table))
    core = lax.axis_index("rcv") % 2
    half_f = half.shape[1]
    quarter = half_f // 2
    cos_t, sin_t = table
    lagged = None
    for q in range(2):
        mine = lax.all_gather(half[:, q * quarter:(q + 1) * quarter], "win", axis=0, tiled=True)
        other = lax.ppermute(mine, "rcv", shifted(1, 2, 1, n))
        for piece, first_f in ((mine, core * half_f), (other, (1 - core) * half_f)):
            first_f = first_f + q * quarter
            rcv_piece = lax.dynamic_slice_in_dim(receivers, first_f, quarter, axis=1)
            flipped = jnp.stack([piece[:, :, 1], -piece[:, :, 0]], axis=2)
            real_part = jnp.einsum(
                "wfcr,wfcs->frs", rcv_piece, piece, preferred_element_type=jnp.float32
            ).astype(jnp.bfloat16)
            imag_part = jnp.einsum(
                "wfcr,wfcs->frs", rcv_piece, flipped, preferred_element_type=jnp.float32
            ).astype(jnp.bfloat16)
            real_part, imag_part = with_layout_constraint(
                (real_part, imag_part), (Layout((0, 1, 2)), Layout((0, 1, 2)))
            )
            cos_p = lax.dynamic_slice_in_dim(cos_t, first_f, quarter, axis=1)
            sin_p = lax.dynamic_slice_in_dim(sin_t, first_f, quarter, axis=1)
            part = jnp.einsum("lf,frs->lrs", cos_p, real_part, preferred_element_type=jnp.float32)
            part = part + jnp.einsum("lf,frs->lrs", sin_p, imag_part, preferred_element_type=jnp.float32)
            lagged = part if lagged is None else lagged + part
    lagged = with_layout_constraint(lagged, Layout((1, 2, 0)))
    return (lagged * lag_scale).astype(jnp.bfloat16).transpose(1, 2, 0)


def solution(mesh):
    in_specs = (P("rcv", "win", None, None), P())
    out_specs = P("rcv", None, "win")
    return jax.shard_map(body, mesh=mesh, in_specs=in_specs, out_specs=out_specs, check_vma=False)
```

```python
import math

import jax
import jax.numpy as jnp
from jax import lax
from jax.experimental.layout import Layout, with_layout_constraint
from jax.sharding import PartitionSpec as P

RCV_DIMS = (("x", 16, 4), ("z_hi", 8, 2), ("y", 2, 4), ("core", 1, 2))


def coord(index, stride, size):
    return (index // stride) % size


def shifted(stride, size, step, n):
    pairs = []
    for i in range(n):
        c = (i // stride) % size
        pairs.append((i, i + (((c + step) % size) - c) * stride))
    return pairs


def ring_broadcast(held, me, root, stride, size, n):
    dist = (coord(me, stride, size) - coord(root, stride, size)) % size
    up = shifted(stride, size, 1, n)
    if size == 2:
        got = lax.ppermute(held, "rcv", up)
        return jnp.where(dist == 1, got, held)
    assert size == 4
    down = shifted(stride, size, -1, n)
    p1, p2 = jnp.split(held, 2, axis=1)
    from_below = lax.ppermute(p1, "rcv", up)
    from_above = lax.ppermute(p2, "rcv", down)
    p1 = jnp.where(dist == 1, from_below, p1)
    p2 = jnp.where(dist == 3, from_above, p2)
    root_here = dist == 0
    from_below = lax.ppermute(jnp.where(root_here, p2, p1), "rcv", up)
    from_above = lax.ppermute(jnp.where(root_here, p1, p2), "rcv", down)
    p1 = jnp.where(dist == 2, from_below, jnp.where(dist == 3, from_above, p1))
    p2 = jnp.where(dist == 1, from_below, jnp.where(dist == 2, from_above, p2))
    return jnp.concatenate([p1, p2], axis=1)


def source_half(block, root):
    n = lax.axis_size("rcv")
    me = lax.axis_index("rcv")
    core = me % 2
    partner = lax.ppermute(block, "rcv", shifted(1, 2, 1, n))
    held = jnp.where(core == root % 2, block, partner)
    halves = held.reshape(held.shape[:1] + (2, held.shape[1] // 2) + held.shape[2:])
    half = lax.dynamic_index_in_dim(halves, core, 1, keepdims=False)
    for name, stride, size in RCV_DIMS[:-1]:
        half = ring_broadcast(half, me, root, stride, size, n)
    return half


def flat_gather(block):
    rows = block.shape[0]
    flat = lax.all_gather(block.reshape(rows, -1), "win", axis=0, tiled=True)
    return flat.reshape((-1,) + block.shape[1:])


def lag_table(n_freqs, lag_start, n_lags):
    freq_index = jnp.arange(n_freqs, dtype=jnp.int32)
    lag_index = jnp.arange(n_lags, dtype=jnp.int32) + lag_start
    phase_index = lag_index[:, None] * freq_index[None, :] % (2 * n_freqs)
    angle = math.pi / n_freqs * phase_index.astype(jnp.float32)
    return jnp.cos(angle).astype(jnp.bfloat16), (-jnp.sin(angle)).astype(jnp.bfloat16)


def body(spectra, source_block):
    root = source_block[0]
    win_count = lax.axis_size("win")
    n = lax.axis_size("rcv")
    n_freqs = spectra.shape[3]
    all_lags = 2 * n_freqs
    my_lags = all_lags // win_count
    lag_scale = 1.0 / math.sqrt(all_lags * spectra.shape[1] * win_count)
    lag_start = lax.axis_index("win") * my_lags - n_freqs
    table = lax.optimization_barrier(lag_table(n_freqs, lag_start, my_lags))

    block = with_layout_constraint(spectra.transpose(1, 3, 2, 0), Layout((0, 1, 2, 3)))
    receivers = flat_gather(block)
    half = source_half(block, root)
    half, receivers, table = lax.optimization_barrier((half, receivers, table))
    half = flat_gather(half)
    other = lax.ppermute(half, "rcv", shifted(1, 2, 1, n))
    first = lax.axis_index("rcv") % 2 == 0
    source = jnp.concatenate(
        [jnp.where(first, half, other), jnp.where(first, other, half)], axis=1
    )

    flipped = jnp.stack([source[:, :, 1], -source[:, :, 0]], axis=2)
    real_part = jnp.einsum(
        "wfcr,wfcs->frs", receivers, source, preferred_element_type=jnp.float32
    ).astype(jnp.bfloat16)
    imag_part = jnp.einsum(
        "wfcr,wfcs->frs", receivers, flipped, preferred_element_type=jnp.float32
    ).astype(jnp.bfloat16)
    real_part, imag_part = with_layout_constraint(
        (real_part, imag_part), (Layout((0, 1, 2)), Layout((0, 1, 2)))
    )
    cos_t, sin_t = table
    lagged = jnp.einsum("lf,frs->lrs", cos_t, real_part, preferred_element_type=jnp.float32)
    lagged = lagged + jnp.einsum("lf,frs->lrs", sin_t, imag_part, preferred_element_type=jnp.float32)
    lagged = with_layout_constraint(lagged, Layout((1, 2, 0)))
    return (lagged * lag_scale).astype(jnp.bfloat16).transpose(1, 2, 0)


def solution(mesh):
    in_specs = (P("rcv", "win", None, None), P())
    out_specs = P("rcv", None, "win")
    return jax.shard_map(body, mesh=mesh, in_specs=in_specs, out_specs=out_specs, check_vma=False)
```

```python
import math

import jax
import jax.numpy as jnp
from jax import lax
from jax.experimental.layout import Layout, with_layout_constraint
from jax.sharding import PartitionSpec as P

RCV_DIMS = (("x", 16, 4), ("z_hi", 8, 2), ("y", 2, 4), ("core", 1, 2))


def coord(index, stride, size):
    return (index // stride) % size


def shifted(stride, size, step, n):
    pairs = []
    for i in range(n):
        c = (i // stride) % size
        pairs.append((i, i + (((c + step) % size) - c) * stride))
    return pairs


def ring_broadcast(held, me, root, stride, size, n):
    dist = (coord(me, stride, size) - coord(root, stride, size)) % size
    up = shifted(stride, size, 1, n)
    if size == 2:
        got = lax.ppermute(held, "rcv", up)
        return jnp.where(dist == 1, got, held)
    assert size == 4
    down = shifted(stride, size, -1, n)
    p1, p2 = jnp.split(held, 2, axis=1)
    from_below = lax.ppermute(p1, "rcv", up)
    from_above = lax.ppermute(p2, "rcv", down)
    p1 = jnp.where(dist == 1, from_below, p1)
    p2 = jnp.where(dist == 3, from_above, p2)
    root_here = dist == 0
    from_below = lax.ppermute(jnp.where(root_here, p2, p1), "rcv", up)
    from_above = lax.ppermute(jnp.where(root_here, p1, p2), "rcv", down)
    p1 = jnp.where(dist == 2, from_below, jnp.where(dist == 3, from_above, p1))
    p2 = jnp.where(dist == 1, from_below, jnp.where(dist == 2, from_above, p2))
    return jnp.concatenate([p1, p2], axis=1)


def source_half(block, root):
    n = lax.axis_size("rcv")
    me = lax.axis_index("rcv")
    core = me % 2
    partner = lax.ppermute(block, "rcv", shifted(1, 2, 1, n))
    held = jnp.where(core == root % 2, block, partner)
    halves = held.reshape(held.shape[:1] + (2, held.shape[1] // 2) + held.shape[2:])
    half = lax.dynamic_index_in_dim(halves, core, 1, keepdims=False)
    for name, stride, size in RCV_DIMS[:-1]:
        half = ring_broadcast(half, me, root, stride, size, n)
    return half


def lag_table(n_freqs, lag_start, n_lags):
    freq_index = jnp.arange(n_freqs, dtype=jnp.int32)
    lag_index = jnp.arange(n_lags, dtype=jnp.int32) + lag_start
    phase_index = lag_index[:, None] * freq_index[None, :] % (2 * n_freqs)
    angle = math.pi / n_freqs * phase_index.astype(jnp.float32)
    return jnp.cos(angle).astype(jnp.bfloat16), (-jnp.sin(angle)).astype(jnp.bfloat16)


def body(spectra, source_block):
    root = source_block[0]
    win_count = lax.axis_size("win")
    n = lax.axis_size("rcv")
    n_freqs = spectra.shape[3]
    all_lags = 2 * n_freqs
    my_lags = all_lags // win_count
    lag_scale = 1.0 / math.sqrt(all_lags * spectra.shape[1] * win_count)
    lag_start = lax.axis_index("win") * my_lags - n_freqs
    table = lax.optimization_barrier(lag_table(n_freqs, lag_start, my_lags))

    block = with_layout_constraint(spectra.transpose(1, 3, 2, 0), Layout((0, 1, 2, 3)))
    receivers = lax.all_gather(block, "win", axis=0, tiled=True)
    half = source_half(block, root)
    half, receivers, table = lax.optimization_barrier((half, receivers, table))
    half = lax.all_gather(half, "win", axis=0, tiled=True)
    as_read = Layout((1, 2, 0, 3))
    flipped = jnp.stack([-receivers[:, :, 1], receivers[:, :, 0]], axis=2)
    receivers, flipped = with_layout_constraint((receivers, flipped), (as_read, as_read))
    half, receivers, flipped = lax.optimization_barrier((half, receivers, flipped))
    other = lax.ppermute(half, "rcv", shifted(1, 2, 1, n))
    first = lax.axis_index("rcv") % 2 == 0
    source = jnp.concatenate(
        [jnp.where(first, half, other), jnp.where(first, other, half)], axis=1
    )

    real_part = jnp.einsum(
        "wfcr,wfcs->frs", receivers, source, preferred_element_type=jnp.float32
    ).astype(jnp.bfloat16)
    imag_part = jnp.einsum(
        "wfcr,wfcs->frs", flipped, source, preferred_element_type=jnp.float32
    ).astype(jnp.bfloat16)
    real_part, imag_part = with_layout_constraint(
        (real_part, imag_part), (Layout((0, 1, 2)), Layout((0, 1, 2)))
    )
    cos_t, sin_t = table
    lagged = jnp.einsum("lf,frs->lrs", cos_t, real_part, preferred_element_type=jnp.float32)
    lagged = lagged + jnp.einsum("lf,frs->lrs", sin_t, imag_part, preferred_element_type=jnp.float32)
    lagged = with_layout_constraint(lagged, Layout((1, 2, 0)))
    return (lagged * lag_scale).astype(jnp.bfloat16).transpose(1, 2, 0)


def solution(mesh):
    in_specs = (P("rcv", "win", None, None), P())
    out_specs = P("rcv", None, "win")
    return jax.shard_map(body, mesh=mesh, in_specs=in_specs, out_specs=out_specs, check_vma=False)
```

```python
import math

import jax
import jax.numpy as jnp
from jax import lax
from jax.experimental.layout import Layout, with_layout_constraint
from jax.sharding import PartitionSpec as P

RCV_DIMS = (("x", 16, 4), ("z_hi", 8, 2), ("y", 2, 4), ("core", 1, 2))


def coord(index, stride, size):
    return (index // stride) % size


def shifted(stride, size, step, n):
    pairs = []
    for i in range(n):
        c = (i // stride) % size
        pairs.append((i, i + (((c + step) % size) - c) * stride))
    return pairs


def ring_broadcast(held, me, root, stride, size, n):
    dist = (coord(me, stride, size) - coord(root, stride, size)) % size
    up = shifted(stride, size, 1, n)
    if size == 2:
        got = lax.ppermute(held, "rcv", up)
        return jnp.where(dist == 1, got, held)
    assert size == 4
    down = shifted(stride, size, -1, n)
    p1, p2 = jnp.split(held, 2, axis=1)
    from_below = lax.ppermute(p1, "rcv", up)
    from_above = lax.ppermute(p2, "rcv", down)
    p1 = jnp.where(dist == 1, from_below, p1)
    p2 = jnp.where(dist == 3, from_above, p2)
    root_here = dist == 0
    from_below = lax.ppermute(jnp.where(root_here, p2, p1), "rcv", up)
    from_above = lax.ppermute(jnp.where(root_here, p1, p2), "rcv", down)
    p1 = jnp.where(dist == 2, from_below, jnp.where(dist == 3, from_above, p1))
    p2 = jnp.where(dist == 1, from_below, jnp.where(dist == 2, from_above, p2))
    return jnp.concatenate([p1, p2], axis=1)


def source_half(block, root):
    n = lax.axis_size("rcv")
    me = lax.axis_index("rcv")
    core = me % 2
    partner = lax.ppermute(block, "rcv", shifted(1, 2, 1, n))
    held = jnp.where(core == root % 2, block, partner)
    halves = held.reshape(held.shape[:1] + (2, held.shape[1] // 2) + held.shape[2:])
    half = lax.dynamic_index_in_dim(halves, core, 1, keepdims=False)
    for name, stride, size in RCV_DIMS[:-1]:
        half = ring_broadcast(half, me, root, stride, size, n)
    return half


def lag_table(n_freqs, lag_start, n_lags):
    freq_index = jnp.arange(n_freqs, dtype=jnp.int32)
    lag_index = jnp.arange(n_lags, dtype=jnp.int32) + lag_start
    phase_index = lag_index[:, None] * freq_index[None, :] % (2 * n_freqs)
    angle = math.pi / n_freqs * phase_index.astype(jnp.float32)
    return jnp.cos(angle).astype(jnp.bfloat16), (-jnp.sin(angle)).astype(jnp.bfloat16)


def body(spectra, source_block):
    root = source_block[0]
    win_count = lax.axis_size("win")
    n = lax.axis_size("rcv")
    n_freqs = spectra.shape[3]
    all_lags = 2 * n_freqs
    my_lags = all_lags // win_count
    lag_scale = 1.0 / math.sqrt(all_lags * spectra.shape[1] * win_count)
    lag_start = lax.axis_index("win") * my_lags - n_freqs
    table = lax.optimization_barrier(lag_table(n_freqs, lag_start, my_lags))

    block = with_layout_constraint(spectra.transpose(1, 3, 2, 0), Layout((0, 1, 2, 3)))
    receivers = lax.all_gather(block, "win", axis=0, tiled=True)
    half = source_half(block, root)
    half, receivers, table = lax.optimization_barrier((half, receivers, table))
    half = lax.all_gather(half, "win", axis=0, tiled=True)
    as_read = Layout((1, 2, 0, 3))
    flipped = jnp.stack([-receivers[:, :, 1], receivers[:, :, 0]], axis=2)
    receivers, flipped = with_layout_constraint((receivers, flipped), (as_read, as_read))
    half, receivers, flipped = lax.optimization_barrier((half, receivers, flipped))
    half = with_layout_constraint(half, as_read)
    other = lax.ppermute(half, "rcv", shifted(1, 2, 1, n))
    first = lax.axis_index("rcv") % 2 == 0
    source = jnp.concatenate(
        [jnp.where(first, half, other), jnp.where(first, other, half)], axis=1
    )

    real_part = jnp.einsum(
        "wfcr,wfcs->frs", receivers, source, preferred_element_type=jnp.float32
    ).astype(jnp.bfloat16)
    imag_part = jnp.einsum(
        "wfcr,wfcs->frs", flipped, source, preferred_element_type=jnp.float32
    ).astype(jnp.bfloat16)
    real_part, imag_part = with_layout_constraint(
        (real_part, imag_part), (Layout((0, 1, 2)), Layout((0, 1, 2)))
    )
    cos_t, sin_t = table
    lagged = jnp.einsum("lf,frs->lrs", cos_t, real_part, preferred_element_type=jnp.float32)
    lagged = lagged + jnp.einsum("lf,frs->lrs", sin_t, imag_part, preferred_element_type=jnp.float32)
    lagged = with_layout_constraint(lagged, Layout((1, 2, 0)))
    return (lagged * lag_scale).astype(jnp.bfloat16).transpose(1, 2, 0)


def solution(mesh):
    in_specs = (P("rcv", "win", None, None), P())
    out_specs = P("rcv", None, "win")
    return jax.shard_map(body, mesh=mesh, in_specs=in_specs, out_specs=out_specs, check_vma=False)
```

```python
import math

import jax
import jax.numpy as jnp
from jax import lax
from jax.experimental.layout import Layout, with_layout_constraint
from jax.sharding import PartitionSpec as P

RCV_DIMS = (("x", 16, 4), ("z_hi", 8, 2), ("y", 2, 4), ("core", 1, 2))


def coord(index, stride, size):
    return (index // stride) % size


def shifted(stride, size, step, n):
    pairs = []
    for i in range(n):
        c = (i // stride) % size
        pairs.append((i, i + (((c + step) % size) - c) * stride))
    return pairs


def ring_broadcast(held, me, root, stride, size, n):
    dist = (coord(me, stride, size) - coord(root, stride, size)) % size
    up = shifted(stride, size, 1, n)
    if size == 2:
        got = lax.ppermute(held, "rcv", up)
        return jnp.where(dist == 1, got, held)
    assert size == 4
    down = shifted(stride, size, -1, n)
    p1, p2 = jnp.split(held, 2, axis=1)
    from_below = lax.ppermute(p1, "rcv", up)
    from_above = lax.ppermute(p2, "rcv", down)
    p1 = jnp.where(dist == 1, from_below, p1)
    p2 = jnp.where(dist == 3, from_above, p2)
    root_here = dist == 0
    from_below = lax.ppermute(jnp.where(root_here, p2, p1), "rcv", up)
    from_above = lax.ppermute(jnp.where(root_here, p1, p2), "rcv", down)
    p1 = jnp.where(dist == 2, from_below, jnp.where(dist == 3, from_above, p1))
    p2 = jnp.where(dist == 1, from_below, jnp.where(dist == 2, from_above, p2))
    return jnp.concatenate([p1, p2], axis=1)


def source_half(block, root):
    n = lax.axis_size("rcv")
    me = lax.axis_index("rcv")
    core = me % 2
    partner = lax.ppermute(block, "rcv", shifted(1, 2, 1, n))
    held = jnp.where(core == root % 2, block, partner)
    halves = held.reshape(held.shape[:1] + (2, held.shape[1] // 2) + held.shape[2:])
    half = lax.dynamic_index_in_dim(halves, core, 1, keepdims=False)
    for name, stride, size in RCV_DIMS[:-1]:
        half = ring_broadcast(half, me, root, stride, size, n)
    return half


def lag_table(n_freqs, lag_start, n_lags):
    freq_index = jnp.arange(n_freqs, dtype=jnp.int32)
    lag_index = jnp.arange(n_lags, dtype=jnp.int32) + lag_start
    phase_index = lag_index[:, None] * freq_index[None, :] % (2 * n_freqs)
    angle = math.pi / n_freqs * phase_index.astype(jnp.float32)
    return jnp.cos(angle).astype(jnp.bfloat16), (-jnp.sin(angle)).astype(jnp.bfloat16)


def body(spectra, source_block):
    root = source_block[0]
    win_count = lax.axis_size("win")
    n = lax.axis_size("rcv")
    n_freqs = spectra.shape[3]
    all_lags = 2 * n_freqs
    my_lags = all_lags // win_count
    lag_scale = 1.0 / math.sqrt(all_lags * spectra.shape[1] * win_count)
    lag_start = lax.axis_index("win") * my_lags - n_freqs
    table = lax.optimization_barrier(lag_table(n_freqs, lag_start, my_lags))

    block = with_layout_constraint(spectra.transpose(1, 3, 2, 0), Layout((0, 1, 2, 3)))
    receivers = lax.all_gather(block, "win", axis=0, tiled=True)
    half = source_half(block, root)
    half, receivers, table = lax.optimization_barrier((half, receivers, table))
    half = lax.all_gather(half, "win", axis=0, tiled=True)
    as_read = Layout((1, 2, 0, 3))
    flipped = jnp.stack([-receivers[:, :, 1], receivers[:, :, 0]], axis=2)
    both = with_layout_constraint(jnp.concatenate([receivers, flipped], axis=3), as_read)
    half, both = lax.optimization_barrier((half, both))
    other = lax.ppermute(half, "rcv", shifted(1, 2, 1, n))
    first = lax.axis_index("rcv") % 2 == 0
    source = jnp.concatenate(
        [jnp.where(first, half, other), jnp.where(first, other, half)], axis=1
    )

    parts = jnp.einsum(
        "wfcr,wfcs->frs", both, source, preferred_element_type=jnp.float32
    ).astype(jnp.bfloat16)
    rows = parts.shape[1] // 2
    real_part, imag_part = parts[:, :rows], parts[:, rows:]
    real_part, imag_part = with_layout_constraint(
        (real_part, imag_part), (Layout((0, 1, 2)), Layout((0, 1, 2)))
    )
    cos_t, sin_t = table
    lagged = jnp.einsum("lf,frs->lrs", cos_t, real_part, preferred_element_type=jnp.float32)
    lagged = lagged + jnp.einsum("lf,frs->lrs", sin_t, imag_part, preferred_element_type=jnp.float32)
    lagged = with_layout_constraint(lagged, Layout((1, 2, 0)))
    return (lagged * lag_scale).astype(jnp.bfloat16).transpose(1, 2, 0)


def solution(mesh):
    in_specs = (P("rcv", "win", None, None), P())
    out_specs = P("rcv", None, "win")
    return jax.shard_map(body, mesh=mesh, in_specs=in_specs, out_specs=out_specs, check_vma=False)
```
